128 devices in a mesh: pipe: 16 (over x_hi, y, core), dp: 8 (over x_lo, z).
Axes of the slice: x: 4 (x_hi: 2, x_lo: 2; x = x_hi * 2 + x_lo), y: 4, z: 4, core: 2. Of those that a mesh axis runs over, the one named last changes fastest.
Arguments:
- inputs: bfloat16 [4, 768, 3072], P(None, 'dp'), may hold values from -24 to 24
- projection: bfloat16 [16, 3072, 3072], P('pipe'), may hold values from -0.109375 to 0.109375
- cotangent: bfloat16 [4, 768, 3072], P(None, 'dp'), may hold values from -6 to 6
Outputs:
- weight_grad: bfloat16 [16, 3072, 3072], P('pipe', 'dp')
The draws below stay inside these ranges and needn't reach their ends.
All inputs are finite; a program needn't handle non-finite values.
Results may differ from the reference program's by a relative error of at most 0.033.
Values may be sent and summed in bfloat16 or wider, within the bound.
No kernel may reach another device: no remote copies, remote signals or barrier semaphores. Data moves between devices by JAX's collectives and lax.ppermute only.
A program may use at most 192 MiB of HBM per device.

```python
import math
import jax
import jax.numpy as jnp
from jax import lax

D = 3072
MICRO = 4
TOK_MB = 96
SECTIONS = 16
TOKENS = 768
N_DP = 8


def draw_inputs(key, part):
    key_base, key_rows, key_cols = jax.random.split(key, 3)
    base_values = jnp.clip(jax.random.normal(key_base, (MICRO, TOKENS, D), jnp.float32), -6.0, 6.0)
    low_scale = 0.3
    high_scale = 3.0
    row_scales = jnp.exp(jax.random.uniform(key_rows, (MICRO, TOKENS, 1), jnp.float32, math.log(low_scale), math.log(high_scale)))
    column_scales = jnp.exp(jax.random.uniform(key_cols, (1, 1, D), jnp.float32, math.log(low_scale), math.log(high_scale)))
    return jnp.clip(base_values * row_scales * column_scales, -24.0, 24.0).astype(jnp.bfloat16)


def levels(own_key, extent, pieces, smallest, top_value):
    loudness, own = 1.0, jax.random.fold_in(own_key, 6)
    for dim, shards_of in pieces:
        heights = jnp.exp(jax.random.uniform(jax.random.fold_in(own, dim), (shards_of,), jnp.float32, smallest / len(pieces), top_value / len(pieces)))
        loudness = loudness * jnp.repeat(heights, extent[dim] // shards_of).reshape([-1 if axis == dim else 1 for axis in range(len(extent))])
    return loudness


def centred(stream_key, extent, spread, limit, cuts=(), held_as=jnp.bfloat16):
    array = jax.random.normal(stream_key, extent, jnp.float32) * spread
    if len(cuts) > 0:
        array = levels(stream_key, extent, cuts, -0.22, 0.18) * array
    return jnp.clip(array, min=-limit, max=limit).astype(held_as)


def setup_inputs(seed: int = 0) -> dict:
    key_list = jax.random.split(jax.random.key(seed), 4)
    return {
        "inputs": draw_inputs(jax.random.fold_in(key_list[3], 71), 0),
        "projection": centred(key_list[1], (SECTIONS, D, D), D ** -0.5, 0.109375, ((0, 16),)),
        "cotangent": centred(key_list[2], (MICRO, TOKENS, D), 1.0, 6.0, ((1, 8),)),
    }


EPSILON = 1e-06

def norm_factor(values):
    floats = values.astype(jnp.float32)
    factor = lax.rsqrt(lax.optimization_barrier(jnp.mean(floats * floats, axis=-1, keepdims=True)) + EPSILON)
    return (floats, factor)

def forward_layer(values, weight):
    floats, factor = norm_factor(values)
    normed = (floats * factor).astype(jnp.bfloat16)
    gate_value = jnp.dot(normed, weight, preferred_element_type=jnp.float32)
    output = (floats + jax.nn.silu(gate_value)).astype(jnp.bfloat16)
    return (output, gate_value)

def backward_layer(values, gate_value, upstream, weight):
    floats, factor = norm_factor(values)
    up_float = upstream.astype(jnp.float32)
    sigma = jax.nn.sigmoid(gate_value)
    slope = (up_float * sigma * (1.0 + gate_value * (1.0 - sigma))).astype(jnp.bfloat16)
    back = jnp.dot(slope, weight.T, preferred_element_type=jnp.float32)
    unit = floats * factor
    down = (up_float + factor * (back - unit * lax.optimization_barrier(jnp.mean(back * unit, axis=-1, keepdims=True)))).astype(jnp.bfloat16)
    normed = (floats * factor).astype(jnp.bfloat16)
    return (down, slope, normed)

def replica_sum(normed, slope):
    left_rows = normed.reshape(MICRO, N_DP, TOK_MB, D).transpose(1, 0, 2, 3).reshape(N_DP, MICRO * TOK_MB, D)
    right_rows = slope.reshape(MICRO, N_DP, TOK_MB, D).transpose(1, 0, 2, 3).reshape(N_DP, MICRO * TOK_MB, D)

    def add_replica(total, pair):
        left_part, right_part = pair
        partial_term = jnp.dot(left_part.T, right_part, preferred_element_type=jnp.float32)
        rounded = lax.optimization_barrier(partial_term.astype(jnp.bfloat16))
        return (total + rounded.astype(jnp.float32), None)
    total, unused = lax.scan(add_replica, jnp.zeros((D, D), jnp.float32), (left_rows, right_rows))
    factor = 1.0 / math.sqrt(MICRO * TOKENS)
    return (total * factor).astype(jnp.bfloat16)

def reference(inputs, projection, cotangent):
    flat_inputs = inputs.reshape(MICRO * TOKENS, D)
    kept_inputs = []
    kept_gates = []
    current = flat_inputs
    for section in range(SECTIONS):
        kept_inputs.append(current)
        current, gate_value = forward_layer(current, projection[section])
        kept_gates.append(gate_value)
    upstream = cotangent.reshape(MICRO * TOKENS, D)
    grads = [None] * SECTIONS
    for section in reversed(range(SECTIONS)):
        down, slope, normed = backward_layer(kept_inputs[section], kept_gates[section], upstream, projection[section])
        grads[section] = replica_sum(normed.reshape(MICRO, TOKENS, D), slope.reshape(MICRO, TOKENS, D))
        upstream = down
    return jnp.stack(grads)
```

```python
import math

import jax
import jax.numpy as jnp
from jax import lax
from jax.experimental.layout import Layout, with_layout_constraint
from jax.sharding import PartitionSpec as P

EPSILON = 1e-06


def from_behind(array, axis, by):
    count = lax.axis_size(axis)
    pairs = [(i, i + by) for i in range(count) if 0 <= i + by < count]
    return lax.ppermute(array, axis, pairs)


def norm_factor(values):
    floats = values.astype(jnp.float32)
    factor = lax.rsqrt(jnp.mean(floats * floats, axis=-1, keepdims=True) + EPSILON)
    return (floats, factor)


def forward_layer(values, weight):
    floats, factor = norm_factor(values)
    normed = (floats * factor).astype(jnp.bfloat16)
    gate_value = jnp.dot(normed, weight, preferred_element_type=jnp.float32)
    output = (floats + jax.nn.silu(gate_value)).astype(jnp.bfloat16)
    return (output, gate_value)


def backward_layer(values, gate_value, upstream, weight_t):
    floats, factor = norm_factor(values)
    up_float = upstream.astype(jnp.float32)
    sigma = jax.nn.sigmoid(gate_value)
    slope = (up_float * sigma * (1.0 + gate_value * (1.0 - sigma))).astype(jnp.bfloat16)
    back = jnp.dot(slope, weight_t, preferred_element_type=jnp.float32)
    unit = floats * factor
    down = (
        up_float + factor * (back - unit * jnp.mean(back * unit, axis=-1, keepdims=True))
    ).astype(jnp.bfloat16)
    return (down, slope)


def on_device(inputs, projection, cotangent):
    weight = projection[0]
    micro, rows_mb, width = inputs.shape
    section = lax.axis_index("pipe")
    sections = lax.axis_size("pipe")
    replicas = lax.axis_size("dp")
    ticks = micro + sections - 1
    kept_inputs = jnp.zeros((micro + 2, rows_mb, width), jnp.bfloat16)
    kept_gates = jnp.zeros((micro + 2, rows_mb, width), jnp.float32)
    incoming = jnp.zeros((rows_mb, width), jnp.bfloat16)
    for tick in range(ticks):
        batch = tick - section
        slot = jnp.clip(batch + 1, 0, micro + 1)
        first = lax.dynamic_index_in_dim(inputs, jnp.clip(batch, 0, micro - 1), 0, keepdims=False)
        source = jnp.where(section == 0, first, incoming)
        output, gate_value = forward_layer(source, weight)
        kept_inputs = lax.dynamic_update_index_in_dim(kept_inputs, source, slot, 0)
        kept_gates = lax.dynamic_update_index_in_dim(kept_gates, gate_value, slot, 0)
        if tick + 1 < ticks:
            incoming = from_behind(output, "pipe", 1)

    weight_t = with_layout_constraint(jnp.transpose(weight), Layout((0, 1)))
    kept_slopes = jnp.zeros((micro + 2, rows_mb, width), jnp.bfloat16)
    incoming = jnp.zeros((rows_mb, width), jnp.bfloat16)
    cols = width // replicas
    grad_rows = jnp.zeros((cols, width), jnp.float32)
    for tick in range(ticks):
        batch = tick - (sections - 1 - section)
        slot = jnp.clip(batch + 1, 0, micro + 1)
        first = lax.dynamic_index_in_dim(cotangent, jnp.clip(batch, 0, micro - 1), 0, keepdims=False)
        source = jnp.where(section == sections - 1, first, incoming)
        stored_input = lax.dynamic_index_in_dim(kept_inputs, slot, 0, keepdims=False)
        stored_gate = lax.dynamic_index_in_dim(kept_gates, slot, 0, keepdims=False)
        down, slope = backward_layer(stored_input, stored_gate, source, weight_t)
        kept_slopes = lax.dynamic_update_index_in_dim(kept_slopes, slope, slot, 0)
        if tick + 1 < ticks:
            incoming = from_behind(down, "pipe", -1)
        done = tick - (sections - 1)
        if done >= 0:
            floats, factor = norm_factor(kept_inputs[done + 1])
            normed = (floats * factor).astype(jnp.bfloat16)
            normed_cols = lax.all_to_all(normed, "dp", 1, 0, tiled=True)
            slope_all = lax.all_gather(kept_slopes[done + 1], "dp", axis=0, tiled=True)
            grad_rows = grad_rows + lax.dot_general(
                normed_cols, slope_all, (((0,), (0,)), ((), ())), preferred_element_type=jnp.float32
            )
    factor_out = 1.0 / math.sqrt(micro * rows_mb * replicas)
    return (grad_rows * factor_out).astype(jnp.bfloat16)[None]


def solution(mesh):
    placed = (P(None, "dp", None), P("pipe", None, None), P(None, "dp", None))
    return jax.shard_map(
        on_device, mesh=mesh, in_specs=placed, out_specs=P("pipe", "dp", None), check_vma=False
    )
```

```python
import math

import jax
import jax.numpy as jnp
from jax import lax
from jax.experimental.layout import Layout, with_layout_constraint
from jax.sharding import PartitionSpec as P

EPSILON = 1e-06


def relay(array, by):
    sections = lax.axis_size("pipe")
    replicas = lax.axis_size("dp")
    middle = sections // 2
    pairs = []
    for section in range(sections):
        target = section + by
        if not 0 <= target < sections:
            continue
        crossing = {section, target} == {middle - 1, middle}
        for replica in range(replicas):
            other = (replica + replicas // 2) % replicas if crossing else replica
            pairs.append((section * replicas + replica, target * replicas + other))
    return lax.ppermute(array, ("pipe", "dp"), pairs)


def norm_factor(values):
    floats = values.astype(jnp.float32)
    factor = lax.rsqrt(jnp.mean(floats * floats, axis=-1, keepdims=True) + EPSILON)
    return (floats, factor)


def forward_layer(values, weight):
    floats, factor = norm_factor(values)
    normed = (floats * factor).astype(jnp.bfloat16)
    gate_value = jnp.dot(normed, weight, preferred_element_type=jnp.float32)
    output = (floats + jax.nn.silu(gate_value)).astype(jnp.bfloat16)
    return (output, gate_value)


def backward_layer(values, gate_value, upstream, weight_t):
    floats, factor = norm_factor(values)
    up_float = upstream.astype(jnp.float32)
    sigma = jax.nn.sigmoid(gate_value)
    slope = (up_float * sigma * (1.0 + gate_value * (1.0 - sigma))).astype(jnp.bfloat16)
    back = jnp.dot(slope, weight_t, preferred_element_type=jnp.float32)
    unit = floats * factor
    down = (
        up_float + factor * (back - unit * jnp.mean(back * unit, axis=-1, keepdims=True))
    ).astype(jnp.bfloat16)
    return (down, slope)


def on_device(inputs, projection, cotangent):
    weight = projection[0]
    micro, rows_mb, width = inputs.shape
    section = lax.axis_index("pipe")
    sections = lax.axis_size("pipe")
    replicas = lax.axis_size("dp")
    ticks = micro + sections - 1
    kept_inputs = jnp.zeros((micro + 2, rows_mb, width), jnp.bfloat16)
    kept_gates = jnp.zeros((micro + 2, rows_mb, width), jnp.float32)
    incoming = jnp.zeros((rows_mb, width), jnp.bfloat16)
    for tick in range(ticks):
        batch = tick - section
        slot = jnp.clip(batch + 1, 0, micro + 1)
        first = lax.dynamic_index_in_dim(inputs, jnp.clip(batch, 0, micro - 1), 0, keepdims=False)
        source = jnp.where(section == 0, first, incoming)
        output, gate_value = forward_layer(source, weight)
        kept_inputs = lax.dynamic_update_index_in_dim(kept_inputs, source, slot, 0)
        kept_gates = lax.dynamic_update_index_in_dim(kept_gates, gate_value, slot, 0)
        if tick + 1 < ticks:
            incoming = relay(output, 1)

    half = replicas // 2
    cotangent = lax.ppermute(cotangent, "dp", [(r, (r + half) % replicas) for r in range(replicas)])
    weight_t = with_layout_constraint(jnp.transpose(weight), Layout((0, 1)))
    kept_slopes = jnp.zeros((micro + 2, rows_mb, width), jnp.bfloat16)
    incoming = jnp.zeros((rows_mb, width), jnp.bfloat16)
    cols = width // replicas
    grad_rows = jnp.zeros((cols, width), jnp.float32)
    for tick in range(ticks):
        batch = tick - (sections - 1 - section)
        slot = jnp.clip(batch + 1, 0, micro + 1)
        first = lax.dynamic_index_in_dim(cotangent, jnp.clip(batch, 0, micro - 1), 0, keepdims=False)
        source = jnp.where(section == sections - 1, first, incoming)
        stored_input = lax.dynamic_index_in_dim(kept_inputs, slot, 0, keepdims=False)
        stored_gate = lax.dynamic_index_in_dim(kept_gates, slot, 0, keepdims=False)
        down, slope = backward_layer(stored_input, stored_gate, source, weight_t)
        kept_slopes = lax.dynamic_update_index_in_dim(kept_slopes, slope, slot, 0)
        if tick + 1 < ticks:
            incoming = relay(down, -1)
        done = tick - (sections - 1)
        if done >= 0:
            floats, factor = norm_factor(kept_inputs[done + 1])
            normed = (floats * factor).astype(jnp.bfloat16)
            normed_cols = lax.all_to_all(normed, "dp", 1, 0, tiled=True)
            finished, kept_slopes = lax.optimization_barrier((kept_slopes[done + 1], kept_slopes))
            slope_all = lax.all_gather(finished, "dp", axis=0, tiled=True)
            grad_rows = grad_rows + lax.dot_general(
                normed_cols, slope_all, (((0,), (0,)), ((), ())), preferred_element_type=jnp.float32
            )
    factor_out = 1.0 / math.sqrt(micro * rows_mb * replicas)
    return (grad_rows * factor_out).astype(jnp.bfloat16)[None]


def solution(mesh):
    placed = (P(None, "dp", None), P("pipe", None, None), P(None, "dp", None))
    return jax.shard_map(
        on_device, mesh=mesh, in_specs=placed, out_specs=P("pipe", "dp", None), check_vma=False
    )
```

```python
import math

import jax
import jax.numpy as jnp
from jax import lax
from jax.sharding import PartitionSpec as P

EPSILON = 1e-06


def relay(array, by):
    sections = lax.axis_size("pipe")
    replicas = lax.axis_size("dp")
    middle = sections // 2
    pairs = []
    for section in range(sections):
        target = section + by
        if not 0 <= target < sections:
            continue
        crossing = {section, target} == {middle - 1, middle}
        for replica in range(replicas):
            other = (replica + replicas // 2) % replicas if crossing else replica
            pairs.append((section * replicas + replica, target * replicas + other))
    return lax.ppermute(array, ("pipe", "dp"), pairs)


def norm_factor(values):
    floats = values.astype(jnp.float32)
    factor = lax.rsqrt(jnp.mean(floats * floats, axis=-1, keepdims=True) + EPSILON)
    return (floats, factor)


def forward_layer(values, weight):
    floats, factor = norm_factor(values)
    normed = (floats * factor).astype(jnp.bfloat16)
    gate_value = jnp.dot(normed, weight, preferred_element_type=jnp.float32)
    output = (floats + jax.nn.silu(gate_value)).astype(jnp.bfloat16)
    return (output, gate_value)


def backward_layer(values, gate_value, upstream, weight_t):
    floats, factor = norm_factor(values)
    up_float = upstream.astype(jnp.float32)
    sigma = jax.nn.sigmoid(gate_value)
    slope = (up_float * sigma * (1.0 + gate_value * (1.0 - sigma))).astype(jnp.bfloat16)
    back = jnp.dot(slope, weight_t, preferred_element_type=jnp.float32)
    unit = floats * factor
    down = (
        up_float + factor * (back - unit * jnp.mean(back * unit, axis=-1, keepdims=True))
    ).astype(jnp.bfloat16)
    return (down, slope)


def on_device(inputs, projection, cotangent):
    weight = projection[0]
    micro, rows_mb, width = inputs.shape
    section = lax.axis_index("pipe")
    sections = lax.axis_size("pipe")
    replicas = lax.axis_size("dp")
    ticks = micro + sections - 1
    kept_inputs = jnp.zeros((micro + 2, rows_mb, width), jnp.bfloat16)
    kept_gates = jnp.zeros((micro + 2, rows_mb, width), jnp.float32)
    incoming = jnp.zeros((rows_mb, width), jnp.bfloat16)
    pieces = sections
    piece = width // pieces
    weight_t = jnp.zeros((width, width), jnp.bfloat16)
    for tick in range(ticks):
        batch = tick - section
        slot = jnp.clip(batch + 1, 0, micro + 1)
        first = lax.dynamic_index_in_dim(inputs, jnp.clip(batch, 0, micro - 1), 0, keepdims=False)
        source = jnp.where(section == 0, first, incoming)
        output, gate_value = forward_layer(source, weight)
        kept_inputs = lax.dynamic_update_index_in_dim(kept_inputs, source, slot, 0)
        kept_gates = lax.dynamic_update_index_in_dim(kept_gates, gate_value, slot, 0)
        if tick + 1 < ticks:
            incoming = relay(output, 1)
        if tick < pieces:
            block = jnp.transpose(lax.slice_in_dim(weight, tick * piece, (tick + 1) * piece, axis=0))
            weight_t = lax.dynamic_update_slice_in_dim(weight_t, block, tick * piece, axis=1)
            weight_t, incoming = lax.optimization_barrier((weight_t, incoming))

    half = replicas // 2
    cotangent = lax.ppermute(cotangent, "dp", [(r, (r + half) % replicas) for r in range(replicas)])
    kept_slopes = jnp.zeros((micro + 2, rows_mb, width), jnp.bfloat16)
    incoming = jnp.zeros((rows_mb, width), jnp.bfloat16)
    cols = width // replicas
    grad_rows = jnp.zeros((cols, width), jnp.float32)
    for tick in range(ticks):
        batch = tick - (sections - 1 - section)
        slot = jnp.clip(batch + 1, 0, micro + 1)
        first = lax.dynamic_index_in_dim(cotangent, jnp.clip(batch, 0, micro - 1), 0, keepdims=False)
        source = jnp.where(section == sections - 1, first, incoming)
        stored_input = lax.dynamic_index_in_dim(kept_inputs, slot, 0, keepdims=False)
        stored_gate = lax.dynamic_index_in_dim(kept_gates, slot, 0, keepdims=False)
        down, slope = backward_layer(stored_input, stored_gate, source, weight_t)
        kept_slopes = lax.dynamic_update_index_in_dim(kept_slopes, slope, slot, 0)
        if tick + 1 < ticks:
            incoming = relay(down, -1)
        done = tick - (sections - 1)
        if done >= 0:
            floats, factor = norm_factor(kept_inputs[done + 1])
            normed = (floats * factor).astype(jnp.bfloat16)
            normed_cols = lax.all_to_all(normed, "dp", 1, 0, tiled=True)
            finished, kept_slopes = lax.optimization_barrier((kept_slopes[done + 1], kept_slopes))
            slope_all = lax.all_gather(finished, "dp", axis=0, tiled=True)
            grad_rows = grad_rows + lax.dot_general(
                normed_cols, slope_all, (((0,), (0,)), ((), ())), preferred_element_type=jnp.float32
            )
    factor_out = 1.0 / math.sqrt(micro * rows_mb * replicas)
    return (grad_rows * factor_out).astype(jnp.bfloat16)[None]


def solution(mesh):
    placed = (P(None, "dp", None), P("pipe", None, None), P(None, "dp", None))
    return jax.shard_map(
        on_device, mesh=mesh, in_specs=placed, out_specs=P("pipe", "dp", None), check_vma=False
    )
```

```python
import math

import jax
import jax.numpy as jnp
from jax import lax
from jax.experimental.layout import Layout, with_layout_constraint
from jax.sharding import PartitionSpec as P

EPSILON = 1e-06


def relay(array, by):
    sections = lax.axis_size("pipe")
    replicas = lax.axis_size("dp")
    middle = sections // 2
    pairs = []
    for section in range(sections):
        target = section + by
        if not 0 <= target < sections:
            continue
        crossing = {section, target} == {middle - 1, middle}
        for replica in range(replicas):
            other = (replica + replicas // 2) % replicas if crossing else replica
            pairs.append((section * replicas + replica, target * replicas + other))
    return lax.ppermute(array, ("pipe", "dp"), pairs)


def norm_factor(values):
    floats = values.astype(jnp.float32)
    factor = lax.rsqrt(jnp.mean(floats * floats, axis=-1, keepdims=True) + EPSILON)
    return (floats, factor)


def forward_layer(values, weight):
    floats, factor = norm_factor(values)
    normed = (floats * factor).astype(jnp.bfloat16)
    gate_value = jnp.dot(normed, weight, preferred_element_type=jnp.float32)
    output = (floats + jax.nn.silu(gate_value)).astype(jnp.bfloat16)
    return (output, gate_value)


def backward_layer(values, gate_value, upstream, weight_t):
    floats, factor = norm_factor(values)
    up_float = upstream.astype(jnp.float32)
    sigma = jax.nn.sigmoid(gate_value)
    slope = (up_float * sigma * (1.0 + gate_value * (1.0 - sigma))).astype(jnp.bfloat16)
    back = jnp.dot(slope, weight_t, preferred_element_type=jnp.float32)
    unit = floats * factor
    down = (
        up_float + factor * (back - unit * jnp.mean(back * unit, axis=-1, keepdims=True))
    ).astype(jnp.bfloat16)
    return (down, slope)


def on_device(inputs, projection, cotangent):
    weight = projection[0]
    micro, rows_mb, width = inputs.shape
    section = lax.axis_index("pipe")
    sections = lax.axis_size("pipe")
    replicas = lax.axis_size("dp")
    ticks = micro + sections - 1
    kept_inputs = jnp.zeros((micro + 2, rows_mb, width), jnp.bfloat16)
    kept_gates = jnp.zeros((micro + 2, rows_mb, width), jnp.float32)
    incoming = jnp.zeros((rows_mb, width), jnp.bfloat16)
    pieces = sections
    piece = width // pieces
    weight_t = with_layout_constraint(jnp.zeros((width, width), jnp.bfloat16), Layout((0, 1)))
    for tick in range(ticks):
        batch = tick - section
        slot = jnp.clip(batch + 1, 0, micro + 1)
        first = lax.dynamic_index_in_dim(inputs, jnp.clip(batch, 0, micro - 1), 0, keepdims=False)
        source = jnp.where(section == 0, first, incoming)
        output, gate_value = forward_layer(source, weight)
        kept_inputs = lax.dynamic_update_index_in_dim(kept_inputs, source, slot, 0)
        kept_gates = lax.dynamic_update_index_in_dim(kept_gates, gate_value, slot, 0)
        if tick + 1 < ticks:
            incoming = relay(output, 1)
        if tick < pieces:
            block = jnp.transpose(lax.slice_in_dim(weight, tick * piece, (tick + 1) * piece, axis=0))
            weight_t = lax.dynamic_update_slice_in_dim(weight_t, block, tick * piece, axis=1)
            weight_t = with_layout_constraint(weight_t, Layout((0, 1)))
            weight_t, incoming = lax.optimization_barrier((weight_t, incoming))

    half = replicas // 2
    cotangent = lax.ppermute(cotangent, "dp", [(r, (r + half) % replicas) for r in range(replicas)])
    kept_slopes = jnp.zeros((micro + 2, rows_mb, width), jnp.bfloat16)
    incoming = jnp.zeros((rows_mb, width), jnp.bfloat16)
    cols = width // replicas
    grad_rows = jnp.zeros((cols, width), jnp.float32)
    for tick in range(ticks):
        batch = tick - (sections - 1 - section)
        slot = jnp.clip(batch + 1, 0, micro + 1)
        first = lax.dynamic_index_in_dim(cotangent, jnp.clip(batch, 0, micro - 1), 0, keepdims=False)
        source = jnp.where(section == sections - 1, first, incoming)
        stored_input = lax.dynamic_index_in_dim(kept_inputs, slot, 0, keepdims=False)
        stored_gate = lax.dynamic_index_in_dim(kept_gates, slot, 0, keepdims=False)
        down, slope = backward_layer(stored_input, stored_gate, source, weight_t)
        kept_slopes = lax.dynamic_update_index_in_dim(kept_slopes, slope, slot, 0)
        if tick + 1 < ticks:
            incoming = relay(down, -1)
        done = tick - (sections - 1)
        if done >= 0:
            floats, factor = norm_factor(kept_inputs[done + 1])
            normed = (floats * factor).astype(jnp.bfloat16)
            normed_cols = lax.all_to_all(normed, "dp", 1, 0, tiled=True)
            finished, kept_slopes = lax.optimization_barrier((kept_slopes[done + 1], kept_slopes))
            slope_all = lax.all_gather(finished, "dp", axis=0, tiled=True)
            grad_rows = grad_rows + lax.dot_general(
                normed_cols, slope_all, (((0,), (0,)), ((), ())), preferred_element_type=jnp.float32
            )
    factor_out = 1.0 / math.sqrt(micro * rows_mb * replicas)
    return (grad_rows * factor_out).astype(jnp.bfloat16)[None]


def solution(mesh):
    placed = (P(None, "dp", None), P("pipe", None, None), P(None, "dp", None))
    return jax.shard_map(
        on_device, mesh=mesh, in_specs=placed, out_specs=P("pipe", "dp", None), check_vma=False
    )
```

```python
import math

import jax
import jax.numpy as jnp
from jax import lax
from jax.experimental.layout import Layout, with_layout_constraint
from jax.sharding import PartitionSpec as P

EPSILON = 1e-06


def relay(array, by):
    sections = lax.axis_size("pipe")
    replicas = lax.axis_size("dp")
    middle = sections // 2
    pairs = []
    for section in range(sections):
        target = section + by
        if not 0 <= target < sections:
            continue
        crossing = {section, target} == {middle - 1, middle}
        for replica in range(replicas):
            other = (replica + replicas // 2) % replicas if crossing else replica
            pairs.append((section * replicas + replica, target * replicas + other))
    return lax.ppermute(array, ("pipe", "dp"), pairs)


def norm_factor(values):
    floats = values.astype(jnp.float32)
    factor = lax.rsqrt(jnp.mean(floats * floats, axis=-1, keepdims=True) + EPSILON)
    return (floats, factor)


def forward_layer(values, weight):
    floats, factor = norm_factor(values)
    normed = (floats * factor).astype(jnp.bfloat16)
    gate_value = jnp.dot(normed, weight, preferred_element_type=jnp.float32)
    output = (floats + jax.nn.silu(gate_value)).astype(jnp.bfloat16)
    return (output, gate_value)


def backward_layer(values, gate_value, upstream, weight_t):
    floats, factor = norm_factor(values)
    up_float = upstream.astype(jnp.float32)
    sigma = jax.nn.sigmoid(gate_value)
    slope = (up_float * sigma * (1.0 + gate_value * (1.0 - sigma))).astype(jnp.bfloat16)
    back = jnp.dot(slope, weight_t, preferred_element_type=jnp.float32)
    unit = floats * factor
    down = (
        up_float + factor * (back - unit * jnp.mean(back * unit, axis=-1, keepdims=True))
    ).astype(jnp.bfloat16)
    return (down, slope)


def on_device(inputs, projection, cotangent):
    weight = projection[0]
    micro, rows_mb, width = inputs.shape
    section = lax.axis_index("pipe")
    sections = lax.axis_size("pipe")
    replicas = lax.axis_size("dp")
    ticks = micro + sections - 1
    kept_inputs = jnp.zeros((micro + 2, rows_mb, width), jnp.bfloat16)
    kept_gates = jnp.zeros((micro + 2, rows_mb, width), jnp.float32)
    incoming = jnp.zeros((rows_mb, width), jnp.bfloat16)
    for tick in range(ticks):
        batch = tick - section
        slot = jnp.clip(batch + 1, 0, micro + 1)
        first = lax.dynamic_index_in_dim(inputs, jnp.clip(batch, 0, micro - 1), 0, keepdims=False)
        source = jnp.where(section == 0, first, incoming)
        output, gate_value = forward_layer(source, weight)
        kept_inputs = lax.dynamic_update_index_in_dim(kept_inputs, source, slot, 0)
        kept_gates = lax.dynamic_update_index_in_dim(kept_gates, gate_value, slot, 0)
        if tick + 1 < ticks:
            incoming = relay(output, 1)

    half = replicas // 2
    cotangent = lax.ppermute(cotangent, "dp", [(r, (r + half) % replicas) for r in range(replicas)])
    weight_t = with_layout_constraint(jnp.transpose(weight), Layout((0, 1)))
    kept_slopes = jnp.zeros((micro + 2, rows_mb, width), jnp.bfloat16)
    incoming = jnp.zeros((rows_mb, width), jnp.bfloat16)
    cols = width // replicas
    ring = replicas // 2
    rep = lax.axis_index("dp")
    side = rep // ring
    place = rep % ring
    partial = jnp.zeros((2 * cols, width), jnp.float32)
    for tick in range(ticks):
        batch = tick - (sections - 1 - section)
        slot = jnp.clip(batch + 1, 0, micro + 1)
        first = lax.dynamic_index_in_dim(cotangent, jnp.clip(batch, 0, micro - 1), 0, keepdims=False)
        source = jnp.where(section == sections - 1, first, incoming)
        stored_input = lax.dynamic_index_in_dim(kept_inputs, slot, 0, keepdims=False)
        stored_gate = lax.dynamic_index_in_dim(kept_gates, slot, 0, keepdims=False)
        down, slope = backward_layer(stored_input, stored_gate, source, weight_t)
        kept_slopes = lax.dynamic_update_index_in_dim(kept_slopes, slope, slot, 0)
        if tick + 1 < ticks:
            incoming = relay(down, -1)
        done = tick - (sections - 1)
        if done >= 0:
            finished, kept_slopes = lax.optimization_barrier((kept_slopes[done + 1], kept_slopes))
            floats, factor = norm_factor(kept_inputs[done + 1])
            normed = (floats * factor).astype(jnp.bfloat16).reshape(rows_mb, replicas, cols)
            slope_rows = []
            normed_rows = []
            for shift in range(ring):
                target = (place + shift) % ring
                wanted = jnp.concatenate(
                    [
                        lax.dynamic_slice_in_dim(normed, target, 1, axis=1),
                        lax.dynamic_slice_in_dim(normed, target + ring, 1, axis=1),
                    ],
                    axis=1,
                )
                if shift == 0:
                    slope_rows.append(finished)
                    normed_rows.append(wanted)
                    continue
                pairs = [
                    (row * ring + r, row * ring + (r + shift) % ring)
                    for row in range(2)
                    for r in range(ring)
                ]
                slope_rows.append(lax.ppermute(finished, "dp", pairs))
                normed_rows.append(lax.ppermute(wanted, "dp", pairs))
            slope_rows = jnp.concatenate(slope_rows, axis=0)
            normed_rows = jnp.concatenate(normed_rows, axis=0).reshape(ring * rows_mb, 2 * cols)
            partial = partial + lax.dot_general(
                normed_rows, slope_rows, (((0,), (0,)), ((), ())), preferred_element_type=jnp.float32
            )
    partial = partial.reshape(2, cols, width)
    mine = lax.dynamic_index_in_dim(partial, side, 0, keepdims=False)
    theirs = lax.dynamic_index_in_dim(partial, 1 - side, 0, keepdims=False).astype(jnp.bfloat16)
    theirs = lax.ppermute(theirs, "dp", [(r, (r + ring) % replicas) for r in range(replicas)])
    factor_out = 1.0 / math.sqrt(micro * rows_mb * replicas)
    return ((mine + theirs.astype(jnp.float32)) * factor_out).astype(jnp.bfloat16)[None]


def solution(mesh):
    placed = (P(None, "dp", None), P("pipe", None, None), P(None, "dp", None))
    return jax.shard_map(
        on_device, mesh=mesh, in_specs=placed, out_specs=P("pipe", "dp", None), check_vma=False
    )
```

```python
import math

import jax
import jax.numpy as jnp
from jax import lax
from jax.experimental.layout import Layout, with_layout_constraint
from jax.sharding import PartitionSpec as P

EPSILON = 1e-06


def relay(array, by):
    sections = lax.axis_size("pipe")
    replicas = lax.axis_size("dp")
    middle = sections // 2
    pairs = []
    for section in range(sections):
        target = section + by
        if not 0 <= target < sections:
            continue
        crossing = {section, target} == {middle - 1, middle}
        for replica in range(replicas):
            other = (replica + replicas // 2) % replicas if crossing else replica
            pairs.append((section * replicas + replica, target * replicas + other))
    return lax.ppermute(array, ("pipe", "dp"), pairs)


def norm_factor(values):
    floats = values.astype(jnp.float32)
    factor = lax.rsqrt(jnp.mean(floats * floats, axis=-1, keepdims=True) + EPSILON)
    return (floats, factor)


def forward_layer(values, weight):
    floats, factor = norm_factor(values)
    normed = (floats * factor).astype(jnp.bfloat16)
    gate_value = jnp.dot(normed, weight, preferred_element_type=jnp.float32)
    output = (floats + jax.nn.silu(gate_value)).astype(jnp.bfloat16)
    return (output, gate_value)


def backward_layer(values, gate_value, upstream, weight_t):
    floats, factor = norm_factor(values)
    up_float = upstream.astype(jnp.float32)
    sigma = jax.nn.sigmoid(gate_value)
    slope = (up_float * sigma * (1.0 + gate_value * (1.0 - sigma))).astype(jnp.bfloat16)
    back = jnp.dot(slope, weight_t, preferred_element_type=jnp.float32)
    unit = floats * factor
    down = (
        up_float + factor * (back - unit * jnp.mean(back * unit, axis=-1, keepdims=True))
    ).astype(jnp.bfloat16)
    return (down, slope)


def on_device(inputs, projection, cotangent):
    weight = projection[0]
    split = 2
    micro, rows_mb, width = inputs.shape
    micro, rows_mb = micro * split, rows_mb // split
    inputs = inputs.reshape(micro, rows_mb, width)
    cotangent = cotangent.reshape(micro, rows_mb, width)
    section = lax.axis_index("pipe")
    sections = lax.axis_size("pipe")
    replicas = lax.axis_size("dp")
    ticks = micro + sections - 1
    kept_inputs = jnp.zeros((micro + 2, rows_mb, width), jnp.bfloat16)
    kept_gates = jnp.zeros((micro + 2, rows_mb, width), jnp.float32)
    incoming = jnp.zeros((rows_mb, width), jnp.bfloat16)
    for tick in range(ticks):
        batch = tick - section
        slot = jnp.clip(batch + 1, 0, micro + 1)
        first = lax.dynamic_index_in_dim(inputs, jnp.clip(batch, 0, micro - 1), 0, keepdims=False)
        source = jnp.where(section == 0, first, incoming)
        output, gate_value = forward_layer(source, weight)
        kept_inputs = lax.dynamic_update_index_in_dim(kept_inputs, source, slot, 0)
        kept_gates = lax.dynamic_update_index_in_dim(kept_gates, gate_value, slot, 0)
        if tick + 1 < ticks:
            incoming = relay(output, 1)

    half = replicas // 2
    cotangent = lax.ppermute(cotangent, "dp", [(r, (r + half) % replicas) for r in range(replicas)])
    weight_t = with_layout_constraint(jnp.transpose(weight), Layout((0, 1)))
    kept_slopes = jnp.zeros((micro + 2, rows_mb, width), jnp.bfloat16)
    incoming = jnp.zeros((rows_mb, width), jnp.bfloat16)
    cols = width // replicas
    ring = replicas // 2
    rep = lax.axis_index("dp")
    side = rep // ring
    place = rep % ring
    partial = jnp.zeros((2 * cols, width), jnp.float32)
    for tick in range(ticks):
        batch = tick - (sections - 1 - section)
        slot = jnp.clip(batch + 1, 0, micro + 1)
        first = lax.dynamic_index_in_dim(cotangent, jnp.clip(batch, 0, micro - 1), 0, keepdims=False)
        source = jnp.where(section == sections - 1, first, incoming)
        stored_input = lax.dynamic_index_in_dim(kept_inputs, slot, 0, keepdims=False)
        stored_gate = lax.dynamic_index_in_dim(kept_gates, slot, 0, keepdims=False)
        down, slope = backward_layer(stored_input, stored_gate, source, weight_t)
        kept_slopes = lax.dynamic_update_index_in_dim(kept_slopes, slope, slot, 0)
        if tick + 1 < ticks:
            incoming = relay(down, -1)
        done = tick - (sections - 1)
        if done >= 0:
            finished, kept_slopes = lax.optimization_barrier((kept_slopes[done + 1], kept_slopes))
            floats, factor = norm_factor(kept_inputs[done + 1])
            normed = (floats * factor).astype(jnp.bfloat16).reshape(rows_mb, replicas, cols)
            slope_rows = []
            normed_rows = []
            for shift in range(ring):
                target = (place + shift) % ring
                wanted = jnp.concatenate(
                    [
                        lax.dynamic_slice_in_dim(normed, target, 1, axis=1),
                        lax.dynamic_slice_in_dim(normed, target + ring, 1, axis=1),
                    ],
                    axis=1,
                )
                if shift == 0:
                    slope_rows.append(finished)
                    normed_rows.append(wanted)
                    continue
                pairs = [
                    (row * ring + r, row * ring + (r + shift) % ring)
                    for row in range(2)
                    for r in range(ring)
                ]
                slope_rows.append(lax.ppermute(finished, "dp", pairs))
                normed_rows.append(lax.ppermute(wanted, "dp", pairs))
            slope_rows = jnp.concatenate(slope_rows, axis=0)
            normed_rows = jnp.concatenate(normed_rows, axis=0).reshape(ring * rows_mb, 2 * cols)
            partial = partial + lax.dot_general(
                normed_rows, slope_rows, (((0,), (0,)), ((), ())), preferred_element_type=jnp.float32
            )
    partial = partial.reshape(2, cols, width)
    mine = lax.dynamic_index_in_dim(partial, side, 0, keepdims=False)
    theirs = lax.dynamic_index_in_dim(partial, 1 - side, 0, keepdims=False).astype(jnp.bfloat16)
    theirs = lax.ppermute(theirs, "dp", [(r, (r + ring) % replicas) for r in range(replicas)])
    factor_out = 1.0 / math.sqrt(micro * rows_mb * replicas)
    return ((mine + theirs.astype(jnp.float32)) * factor_out).astype(jnp.bfloat16)[None]


def solution(mesh):
    placed = (P(None, "dp", None), P("pipe", None, None), P(None, "dp", None))
    return jax.shard_map(
        on_device, mesh=mesh, in_specs=placed, out_specs=P("pipe", "dp", None), check_vma=False
    )
```

```python
import math

import jax
import jax.numpy as jnp
from jax import lax
from jax.experimental.layout import Layout, with_layout_constraint
from jax.sharding import PartitionSpec as P

EPSILON = 1e-06


def relay(array, by):
    sections = lax.axis_size("pipe")
    replicas = lax.axis_size("dp")
    middle = sections // 2
    pairs = []
    for section in range(sections):
        target = section + by
        if not 0 <= target < sections:
            continue
        crossing = {section, target} == {middle - 1, middle}
        for replica in range(replicas):
            other = (replica + replicas // 2) % replicas if crossing else replica
            pairs.append((section * replicas + replica, target * replicas + other))
    return lax.ppermute(array, ("pipe", "dp"), pairs)


def norm_factor(values):
    floats = values.astype(jnp.float32)
    factor = lax.rsqrt(jnp.mean(floats * floats, axis=-1, keepdims=True) + EPSILON)
    return (floats, factor)


def forward_layer(values, weight):
    floats, factor = norm_factor(values)
    normed = (floats * factor).astype(jnp.bfloat16)
    gate_value = jnp.dot(normed, weight, preferred_element_type=jnp.float32)
    output = (floats + jax.nn.silu(gate_value)).astype(jnp.bfloat16)
    return (output, gate_value)


def backward_layer(values, gate_value, upstream, weight_t):
    floats, factor = norm_factor(values)
    up_float = upstream.astype(jnp.float32)
    sigma = jax.nn.sigmoid(gate_value)
    slope = (up_float * sigma * (1.0 + gate_value * (1.0 - sigma))).astype(jnp.bfloat16)
    back = jnp.dot(slope, weight_t, preferred_element_type=jnp.float32)
    unit = floats * factor
    down = (
        up_float + factor * (back - unit * jnp.mean(back * unit, axis=-1, keepdims=True))
    ).astype(jnp.bfloat16)
    return (down, slope)


def on_device(inputs, projection, cotangent):
    weight = projection[0]
    micro, rows_mb, width = inputs.shape
    section = lax.axis_index("pipe")
    sections = lax.axis_size("pipe")
    replicas = lax.axis_size("dp")
    ticks = micro + sections - 1
    kept_inputs = jnp.zeros((micro + 2, rows_mb, width), jnp.bfloat16)
    kept_gates = jnp.zeros((micro + 2, rows_mb, width), jnp.float32)
    incoming = jnp.zeros((rows_mb, width), jnp.bfloat16)
    for tick in range(ticks):
        batch = tick - section
        slot = jnp.clip(batch + 1, 0, micro + 1)
        first = lax.dynamic_index_in_dim(inputs, jnp.clip(batch, 0, micro - 1), 0, keepdims=False)
        source = jnp.where(section == 0, first, incoming)
        output, gate_value = forward_layer(source, weight)
        kept_inputs = lax.dynamic_update_index_in_dim(kept_inputs, source, slot, 0)
        kept_gates = lax.dynamic_update_index_in_dim(kept_gates, gate_value, slot, 0)
        if tick + 1 < ticks:
            incoming = relay(output, 1)

    half = replicas // 2
    cotangent = lax.ppermute(cotangent, "dp", [(r, (r + half) % replicas) for r in range(replicas)])
    weight_t = with_layout_constraint(jnp.transpose(weight), Layout((0, 1)))
    split = 2
    kept_inputs = kept_inputs.reshape(split * (micro + 2), rows_mb // split, width)
    kept_gates = kept_gates.reshape(split * (micro + 2), rows_mb // split, width)
    micro, rows_mb = micro * split, rows_mb // split
    cotangent = cotangent.reshape(micro, rows_mb, width)
    ticks = micro + sections - 1
    kept_slopes = jnp.zeros((micro + 2, rows_mb, width), jnp.bfloat16)
    incoming = jnp.zeros((rows_mb, width), jnp.bfloat16)
    cols = width // replicas
    ring = replicas // 2
    rep = lax.axis_index("dp")
    side = rep // ring
    place = rep % ring
    mine = jnp.zeros((cols, width), jnp.float32)
    theirs = jnp.zeros((cols, width), jnp.float32)
    for tick in range(ticks):
        batch = tick - (sections - 1 - section)
        slot = jnp.clip(batch + 1, 0, micro + 1)
        first = lax.dynamic_index_in_dim(cotangent, jnp.clip(batch, 0, micro - 1), 0, keepdims=False)
        source = jnp.where(section == sections - 1, first, incoming)
        stored = jnp.clip(batch + split, 0, split * (micro // split + 2) - 1)
        stored_input = lax.dynamic_index_in_dim(kept_inputs, stored, 0, keepdims=False)
        stored_gate = lax.dynamic_index_in_dim(kept_gates, stored, 0, keepdims=False)
        down, slope = backward_layer(stored_input, stored_gate, source, weight_t)
        kept_slopes = lax.dynamic_update_index_in_dim(kept_slopes, slope, slot, 0)
        if tick + 1 < ticks:
            incoming = relay(down, -1)
        done = tick - (sections - 1)
        if done >= 0:
            finished, kept_slopes = lax.optimization_barrier((kept_slopes[done + 1], kept_slopes))
            floats, factor = norm_factor(kept_inputs[done + split])
            normed = (floats * factor).astype(jnp.bfloat16).reshape(rows_mb, replicas, cols)
            slope_rows = []
            normed_rows = []
            for shift in range(ring):
                target = (place + shift) % ring
                wanted = jnp.concatenate(
                    [
                        lax.dynamic_slice_in_dim(normed, target, 1, axis=1),
                        lax.dynamic_slice_in_dim(normed, target + ring, 1, axis=1),
                    ],
                    axis=1,
                )
                if shift == 0:
                    slope_rows.append(finished)
                    normed_rows.append(wanted)
                    continue
                pairs = [
                    (row * ring + r, row * ring + (r + shift) % ring)
                    for row in range(2)
                    for r in range(ring)
                ]
                slope_rows.append(lax.ppermute(finished, "dp", pairs))
                normed_rows.append(lax.ppermute(wanted, "dp", pairs))
            slope_rows = jnp.concatenate(slope_rows, axis=0)
            normed_rows = jnp.concatenate(normed_rows, axis=0)
            contract = (((0,), (0,)), ((), ()))
            theirs = theirs + lax.dot_general(
                lax.dynamic_index_in_dim(normed_rows, 1 - side, 1, keepdims=False),
                slope_rows, contract, preferred_element_type=jnp.float32,
            )
            mine = mine + lax.dot_general(
                lax.dynamic_index_in_dim(normed_rows, side, 1, keepdims=False),
                slope_rows, contract, preferred_element_type=jnp.float32,
            )
    theirs = lax.ppermute(
        theirs.astype(jnp.bfloat16), "dp", [(r, (r + ring) % replicas) for r in range(replicas)]
    )
    factor_out = 1.0 / math.sqrt(micro * rows_mb * replicas)
    return ((mine + theirs.astype(jnp.float32)) * factor_out).astype(jnp.bfloat16)[None]


def solution(mesh):
    placed = (P(None, "dp", None), P("pipe", None, None), P(None, "dp", None))
    return jax.shard_map(
        on_device, mesh=mesh, in_specs=placed, out_specs=P("pipe", "dp", None), check_vma=False
    )
```

```python
import math

import jax
import jax.numpy as jnp
from jax import lax
from jax.experimental.layout import Layout, with_layout_constraint
from jax.sharding import PartitionSpec as P

EPSILON = 1e-06


def relay(array, by):
    sections = lax.axis_size("pipe")
    replicas = lax.axis_size("dp")
    middle = sections // 2
    pairs = []
    for section in range(sections):
        target = section + by
        if not 0 <= target < sections:
            continue
        crossing = {section, target} == {middle - 1, middle}
        for replica in range(replicas):
            other = (replica + replicas // 2) % replicas if crossing else replica
            pairs.append((section * replicas + replica, target * replicas + other))
    return lax.ppermute(array, ("pipe", "dp"), pairs)


def norm_factor(values):
    floats = values.astype(jnp.float32)
    factor = lax.rsqrt(jnp.mean(floats * floats, axis=-1, keepdims=True) + EPSILON)
    return (floats, factor)


def forward_layer(values, weight):
    floats, factor = norm_factor(values)
    normed = (floats * factor).astype(jnp.bfloat16)
    gate_value = jnp.dot(normed, weight, preferred_element_type=jnp.float32)
    output = (floats + jax.nn.silu(gate_value)).astype(jnp.bfloat16)
    return (output, gate_value)


def backward_layer(values, gate_value, upstream, weight_t):
    floats, factor = norm_factor(values)
    up_float = upstream.astype(jnp.float32)
    sigma = jax.nn.sigmoid(gate_value)
    slope = (up_float * sigma * (1.0 + gate_value * (1.0 - sigma))).astype(jnp.bfloat16)
    back = jnp.dot(slope, weight_t, preferred_element_type=jnp.float32)
    unit = floats * factor
    down = (
        up_float + factor * (back - unit * jnp.mean(back * unit, axis=-1, keepdims=True))
    ).astype(jnp.bfloat16)
    return (down, slope)


def on_device(inputs, projection, cotangent):
    weight = projection[0]
    split = 2
    micro, rows_mb, width = inputs.shape
    micro, rows_mb = micro * split, rows_mb // split
    inputs = inputs.reshape(micro, rows_mb, width)
    cotangent = cotangent.reshape(micro, rows_mb, width)
    section = lax.axis_index("pipe")
    sections = lax.axis_size("pipe")
    replicas = lax.axis_size("dp")
    ticks = micro + sections - 1
    kept_inputs = jnp.zeros((micro + 2, rows_mb, width), jnp.bfloat16)
    kept_gates = jnp.zeros((micro + 2, rows_mb, width), jnp.float32)
    incoming = jnp.zeros((rows_mb, width), jnp.bfloat16)
    for tick in range(ticks):
        batch = tick - section
        slot = jnp.clip(batch + 1, 0, micro + 1)
        first = lax.dynamic_index_in_dim(inputs, jnp.clip(batch, 0, micro - 1), 0, keepdims=False)
        source = jnp.where(section == 0, first, incoming)
        output, gate_value = forward_layer(source, weight)
        kept_inputs = lax.dynamic_update_index_in_dim(kept_inputs, source, slot, 0)
        kept_gates = lax.dynamic_update_index_in_dim(kept_gates, gate_value, slot, 0)
        if tick + 1 < ticks:
            incoming = relay(output, 1)

    half = replicas // 2
    cotangent = lax.ppermute(cotangent, "dp", [(r, (r + half) % replicas) for r in range(replicas)])
    weight_t = with_layout_constraint(jnp.transpose(weight), Layout((0, 1)))
    kept_slopes = jnp.zeros((micro + 2, rows_mb, width), jnp.bfloat16)
    incoming = jnp.zeros((rows_mb, width), jnp.bfloat16)
    cols = width // replicas
    ring = replicas // 2
    rep = lax.axis_index("dp")
    side = rep // ring
    place = rep % ring
    mine = jnp.zeros((cols, width), jnp.float32)
    theirs = jnp.zeros((cols, width), jnp.float32)
    for tick in range(ticks):
        batch = tick - (sections - 1 - section)
        slot = jnp.clip(batch + 1, 0, micro + 1)
        first = lax.dynamic_index_in_dim(cotangent, jnp.clip(batch, 0, micro - 1), 0, keepdims=False)
        source = jnp.where(section == sections - 1, first, incoming)
        stored_input = lax.dynamic_index_in_dim(kept_inputs, slot, 0, keepdims=False)
        stored_gate = lax.dynamic_index_in_dim(kept_gates, slot, 0, keepdims=False)
        down, slope = backward_layer(stored_input, stored_gate, source, weight_t)
        kept_slopes = lax.dynamic_update_index_in_dim(kept_slopes, slope, slot, 0)
        if tick + 1 < ticks:
            incoming = relay(down, -1)
        done = tick - (sections - 1)
        if done >= 0:
            finished, kept_slopes = lax.optimization_barrier((kept_slopes[done + 1], kept_slopes))
            floats, factor = norm_factor(kept_inputs[done + 1])
            normed = (floats * factor).astype(jnp.bfloat16).reshape(rows_mb, replicas, cols)
            slope_rows = []
            normed_rows = []
            for shift in range(ring):
                target = (place + shift) % ring
                wanted = jnp.concatenate(
                    [
                        lax.dynamic_slice_in_dim(normed, target, 1, axis=1),
                        lax.dynamic_slice_in_dim(normed, target + ring, 1, axis=1),
                    ],
                    axis=1,
                )
                if shift == 0:
                    slope_rows.append(finished)
                    normed_rows.append(wanted)
                    continue
                pairs = [
                    (row * ring + r, row * ring + (r + shift) % ring)
                    for row in range(2)
                    for r in range(ring)
                ]
                slope_rows.append(lax.ppermute(finished, "dp", pairs))
                normed_rows.append(lax.ppermute(wanted, "dp", pairs))
            slope_rows = jnp.concatenate(slope_rows, axis=0)
            normed_rows = jnp.concatenate(normed_rows, axis=0)
            contract = (((0,), (0,)), ((), ()))
            theirs = theirs + lax.dot_general(
                lax.dynamic_index_in_dim(normed_rows, 1 - side, 1, keepdims=False),
                slope_rows, contract, preferred_element_type=jnp.float32,
            )
            mine = mine + lax.dot_general(
                lax.dynamic_index_in_dim(normed_rows, side, 1, keepdims=False),
                slope_rows, contract, preferred_element_type=jnp.float32,
            )
    theirs = lax.ppermute(
        theirs.astype(jnp.bfloat16), "dp", [(r, (r + ring) % replicas) for r in range(replicas)]
    )
    factor_out = 1.0 / math.sqrt(micro * rows_mb * replicas)
    return ((mine + theirs.astype(jnp.float32)) * factor_out).astype(jnp.bfloat16)[None]


def solution(mesh):
    placed = (P(None, "dp", None), P("pipe", None, None), P(None, "dp", None))
    return jax.shard_map(
        on_device, mesh=mesh, in_specs=placed, out_specs=P("pipe", "dp", None), check_vma=False
    )
```

```python
import math

import jax
import jax.numpy as jnp
from jax import lax
from jax.experimental.layout import Layout, with_layout_constraint
from jax.sharding import PartitionSpec as P

EPSILON = 1e-06


def relay(array, by):
    sections = lax.axis_size("pipe")
    replicas = lax.axis_size("dp")
    middle = sections // 2
    pairs = []
    for section in range(sections):
        target = section + by
        if not 0 <= target < sections:
            continue
        crossing = {section, target} == {middle - 1, middle}
        for replica in range(replicas):
            other = (replica + replicas // 2) % replicas if crossing else replica
            pairs.append((section * replicas + replica, target * replicas + other))
    return lax.ppermute(array, ("pipe", "dp"), pairs)


def norm_factor(values):
    floats = values.astype(jnp.float32)
    factor = lax.rsqrt(jnp.mean(floats * floats, axis=-1, keepdims=True) + EPSILON)
    return (floats, factor)


def forward_layer(values, weight):
    floats, factor = norm_factor(values)
    normed = (floats * factor).astype(jnp.bfloat16)
    gate_value = jnp.dot(normed, weight, preferred_element_type=jnp.float32)
    output = (floats + jax.nn.silu(gate_value)).astype(jnp.bfloat16)
    return (output, gate_value)


def backward_layer(values, gate_value, upstream, weight_t):
    floats, factor = norm_factor(values)
    up_float = upstream.astype(jnp.float32)
    sigma = jax.nn.sigmoid(gate_value)
    slope = (up_float * sigma * (1.0 + gate_value * (1.0 - sigma))).astype(jnp.bfloat16)
    back = jnp.dot(slope, weight_t, preferred_element_type=jnp.float32)
    unit = floats * factor
    down = (
        up_float + factor * (back - unit * jnp.mean(back * unit, axis=-1, keepdims=True))
    ).astype(jnp.bfloat16)
    return (down, slope)


def on_device(inputs, projection, cotangent):
    weight = projection[0]
    split = 2
    micro, rows_mb, width = inputs.shape
    micro, rows_mb = micro * split, rows_mb // split
    inputs = inputs.reshape(micro, rows_mb, width)
    cotangent = cotangent.reshape(micro, rows_mb, width)
    section = lax.axis_index("pipe")
    sections = lax.axis_size("pipe")
    replicas = lax.axis_size("dp")
    ticks = micro + sections - 1
    kept_inputs = jnp.zeros((micro + 2, rows_mb, width), jnp.bfloat16)
    kept_gates = jnp.zeros((micro + 2, rows_mb, width), jnp.float32)
    incoming = jnp.zeros((rows_mb, width), jnp.bfloat16)
    for tick in range(ticks):
        batch = tick - section
        slot = jnp.clip(batch + 1, 0, micro + 1)
        first = lax.dynamic_index_in_dim(inputs, jnp.clip(batch, 0, micro - 1), 0, keepdims=False)
        source = jnp.where(section == 0, first, incoming)
        output, gate_value = forward_layer(source, weight)
        kept_inputs = lax.dynamic_update_index_in_dim(kept_inputs, source, slot, 0)
        kept_gates = lax.dynamic_update_index_in_dim(kept_gates, gate_value, slot, 0)
        if tick + 1 < ticks:
            incoming = relay(output, 1)

    half = replicas // 2
    cotangent = lax.ppermute(cotangent, "dp", [(r, (r + half) % replicas) for r in range(replicas)])
    weight_t = with_layout_constraint(jnp.transpose(weight), Layout((0, 1)))
    kept_slopes = jnp.zeros((micro + 2, rows_mb, width), jnp.bfloat16)
    incoming = jnp.zeros((rows_mb, width), jnp.bfloat16)
    cols = width // replicas
    ring = replicas // 2
    rep = lax.axis_index("dp")
    side = rep // ring
    place = rep % ring
    partial = jnp.zeros((2 * cols, width), jnp.float32)
    pending_slopes, pending_normed = [], []
    for tick in range(ticks):
        batch = tick - (sections - 1 - section)
        slot = jnp.clip(batch + 1, 0, micro + 1)
        first = lax.dynamic_index_in_dim(cotangent, jnp.clip(batch, 0, micro - 1), 0, keepdims=False)
        source = jnp.where(section == sections - 1, first, incoming)
        stored_input = lax.dynamic_index_in_dim(kept_inputs, slot, 0, keepdims=False)
        stored_gate = lax.dynamic_index_in_dim(kept_gates, slot, 0, keepdims=False)
        down, slope = backward_layer(stored_input, stored_gate, source, weight_t)
        kept_slopes = lax.dynamic_update_index_in_dim(kept_slopes, slope, slot, 0)
        if tick + 1 < ticks:
            incoming = relay(down, -1)
        done = tick - (sections - 1)
        if done >= 0:
            finished, kept_slopes = lax.optimization_barrier((kept_slopes[done + 1], kept_slopes))
            floats, factor = norm_factor(kept_inputs[done + 1])
            normed = (floats * factor).astype(jnp.bfloat16).reshape(rows_mb, replicas, cols)
            slope_rows = []
            normed_rows = []
            for shift in range(ring):
                target = (place + shift) % ring
                wanted = jnp.concatenate(
                    [
                        lax.dynamic_slice_in_dim(normed, target, 1, axis=1),
                        lax.dynamic_slice_in_dim(normed, target + ring, 1, axis=1),
                    ],
                    axis=1,
                )
                if shift == 0:
                    slope_rows.append(finished)
                    normed_rows.append(wanted)
                    continue
                pairs = [
                    (row * ring + r, row * ring + (r + shift) % ring)
                    for row in range(2)
                    for r in range(ring)
                ]
                slope_rows.append(lax.ppermute(finished, "dp", pairs))
                normed_rows.append(lax.ppermute(wanted, "dp", pairs))
            pending_slopes += slope_rows
            pending_normed += normed_rows
            if done % split == split - 1 or done == micro - 1:
                slope_rows = jnp.concatenate(pending_slopes, axis=0)
                normed_rows = jnp.concatenate(pending_normed, axis=0)
                normed_rows = normed_rows.reshape(normed_rows.shape[0], 2 * cols)
                partial = partial + lax.dot_general(
                    normed_rows, slope_rows, (((0,), (0,)), ((), ())), preferred_element_type=jnp.float32
                )
                pending_slopes, pending_normed = [], []
    partial = partial.reshape(2, cols, width)
    mine = lax.dynamic_index_in_dim(partial, side, 0, keepdims=False)
    theirs = lax.dynamic_index_in_dim(partial, 1 - side, 0, keepdims=False).astype(jnp.bfloat16)
    theirs = lax.ppermute(theirs, "dp", [(r, (r + ring) % replicas) for r in range(replicas)])
    factor_out = 1.0 / math.sqrt(micro * rows_mb * replicas)
    return ((mine + theirs.astype(jnp.float32)) * factor_out).astype(jnp.bfloat16)[None]


def solution(mesh):
    placed = (P(None, "dp", None), P("pipe", None, None), P(None, "dp", None))
    return jax.shard_map(
        on_device, mesh=mesh, in_specs=placed, out_specs=P("pipe", "dp", None), check_vma=False
    )
```
